1024 devices in a mesh: blk: 16 (over x, core), rep: 64 (over z, y).
Axes of the slice: x: 8, y: 8, z: 8, core: 2. Of those that a mesh axis runs over, the one named last changes fastest.
Arguments:
- features: bfloat16 [2048, 128, 256], P(('blk', 'rep')), may hold values from -6 to 6
- weight: bfloat16 [256, 256], replicated, may hold values from -0.375 to 0.375
- tile_values: bfloat16 [2048, 24, 128, 128], P(('blk', 'rep')), may hold values from -0.1875 to 0.1875
- tile_count: int32 [2048], P(('blk', 'rep')), may hold values from 1 to 24, as said below
- tile_cols: int32 [2048, 24], P(('blk', 'rep')), may hold values from 0 to 2047, as said below
- out_grad: bfloat16 [2048, 128, 256], P(('blk', 'rep')), may hold values from -6 to 6
- relu_mask: int32 [2048, 128, 256], P(('blk', 'rep')), may hold values 0 or 1
Outputs:
- activated: bfloat16 [2048, 128, 256], P(('blk', 'rep'))
- weight_grad: float32 [256, 256], replicated
- in_grad: bfloat16 [2048, 128, 256], P(('blk', 'rep'))
The draws below stay inside these ranges and needn't reach their ends.
Inputs may be any that keep to these rules, and one draw needn't show every extreme that they name: `tile_count`: all 2 tile rows of some aligned block of 2 tile rows hold 24 tiles; some tile row holds one. `tile_cols`: tile rows form 64 communities: tile row t belongs to community t // 2 % 64, and every column tile of a tile row lies in its own community; the 24 column tiles of one tile row are distinct; slots not in use hold column tiles too.
All inputs are finite; a program needn't handle non-finite values. No bound on the sum of `relu_mask` on one device may be relied on, other than what follows from the above.
Results may differ from the reference program's by a relative error of at most 0.0049.
Values may be sent and summed in bfloat16 or wider, within the bound.
No kernel may reach another device: no remote copies, remote signals or barrier semaphores. Data moves between devices by JAX's collectives and lax.ppermute only.
A program may use at most 32 MiB of HBM per device.

```python
import math
import jax
import jax.numpy as jnp
from jax import lax

F = 256
TILE = 128
TRD = 2
TROWS = 2048
COMM = 32
SLOTS = 24
N_REP = 64


def draw_tile_count(key, part):
    block_total = TROWS // TRD
    hot_block = jax.random.randint(jax.random.fold_in(key, 11), (), 0, block_total)
    base_count = jax.random.randint(jax.random.fold_in(key, 12), (TROWS,), 1, 16)
    row_index = jnp.arange(TROWS, dtype=jnp.int32)
    counts = jnp.where(row_index // TRD == hot_block, SLOTS, jnp.minimum(base_count, SLOTS))
    single_row = (hot_block + 1) % block_total * TRD
    counts = jnp.where(row_index == single_row, 1, counts)
    return counts.astype(jnp.int32)


def draw_tile_cols(key, part):
    scores = jax.random.randint(jax.random.fold_in(key, 21), (TROWS, COMM), 0, 65536)
    scores = scores * COMM + jnp.arange(COMM, dtype=jnp.int32)[None, :]
    ranked = jnp.argsort(scores, axis=1, stable=True)[:, :SLOTS].astype(jnp.int32)
    row_index = jnp.arange(TROWS, dtype=jnp.int32)
    community = row_index // TRD % N_REP
    columns = (ranked // TRD * N_REP + community[:, None]) * TRD + ranked % TRD
    return columns.astype(jnp.int32)


def with_ends(entries, own_key, smallest, top_value):
    index_at = [jax.random.randint(jax.random.fold_in(own_key, axis), (), 0, length) for axis, length in enumerate(entries.shape)]
    longest = entries.shape.index(max(entries.shape))
    next_to = index_at[:longest] + [(index_at[longest] + 1) % entries.shape[longest]] + index_at[longest + 1:]
    return entries.at[tuple(index_at)].set(smallest).at[tuple(next_to)].set(top_value)


def level_of(key, extent, shards, low, largest):
    loudness, own = 1.0, jax.random.fold_in(key, 6)
    for position, blocks in shards:
        draws = jnp.exp(jax.random.uniform(jax.random.fold_in(own, position), (blocks,), jnp.float32, low / len(shards), largest / len(shards)))
        loudness = loudness * jnp.repeat(draws, extent[position] // blocks).reshape([-1 if axis == position else 1 for axis in range(len(extent))])
    return loudness


def noise(rng, dims, spread, limit, cuts=(), kind=jnp.bfloat16):
    entries = spread * jax.random.normal(rng, dims, jnp.float32)
    if cuts:
        entries = entries * level_of(rng, dims, cuts, -0.22, 0.18)
    return jnp.clip(entries, -limit, limit).astype(kind)


def setup_inputs(seed: int = 0) -> dict:
    splits = jax.random.split(jax.random.key(seed), 8)
    return {
        "features": noise(splits[0], (TROWS, TILE, F), 1.0, 6.0, ((0, 1024),)),
        "weight": noise(splits[1], (F, F), F ** -0.5, 0.375),
        "tile_values": noise(splits[2], (TROWS, SLOTS, TILE, TILE), (TILE * 8) ** -0.5, 0.1875, ((0, 1024),)),
        "tile_count": draw_tile_count(jax.random.fold_in(splits[7], 71), 0),
        "tile_cols": draw_tile_cols(jax.random.fold_in(splits[7], 71), 0),
        "out_grad": noise(splits[5], (TROWS, TILE, F), 1.0, 6.0, ((0, 1024),)),
        "relu_mask": with_ends((jax.random.randint(splits[6], (TROWS, TILE, F), 0, 2) < 1).astype(jnp.int32), jax.random.fold_in(splits[6], 1), 0, 1),
    }


def reference(features, weight, tile_values, tile_count, tile_cols, out_grad, relu_mask):
    in_use = jnp.arange(SLOTS, dtype=jnp.int32)[None, :] < tile_count[:, None]
    masked = jnp.where(in_use[:, :, None, None], tile_values, jnp.zeros_like(tile_values))

    def forward_row(row_pair):
        tile_block, columns = row_pair
        picked = features[columns].astype(jnp.float32)
        return jnp.einsum('sji,sjf->if', tile_block.astype(jnp.float32), picked)
    aggregate = lax.map(forward_row, (masked, tile_cols)).astype(jnp.bfloat16)
    hidden_flat = aggregate.reshape(-1, F)
    linear = jnp.dot(hidden_flat, weight, preferred_element_type=jnp.float32)
    activated = jnp.maximum(linear, 0.0).astype(jnp.bfloat16).reshape(aggregate.shape)
    grad_flat = out_grad.reshape(-1, F)
    grad_scale = 1.0 / math.sqrt(TROWS * TILE)
    weight_grad = jnp.dot(hidden_flat.T, grad_flat, preferred_element_type=jnp.float32) * grad_scale
    row_grad = jnp.dot(grad_flat, weight.T, preferred_element_type=jnp.float32).astype(jnp.bfloat16)
    row_grad = row_grad.reshape(out_grad.shape)

    def backward_row(accum_grad, row_triple):
        tile_block, columns, grads = row_triple
        contrib = jnp.einsum('sji,if->sjf', tile_block.astype(jnp.float32), grads.astype(jnp.float32))
        return (accum_grad.at[columns].add(contrib), None)
    start_grad = jnp.zeros((TROWS, TILE, F), jnp.float32)
    column_grad, _ = lax.scan(backward_row, start_grad, (masked, tile_cols, row_grad))
    in_grad = (relu_mask.astype(jnp.float32) * column_grad).astype(jnp.bfloat16)
    return (activated, weight_grad, in_grad)
```

```python
import math

import jax
import jax.numpy as jnp
from jax import lax
from jax.sharding import PartitionSpec as P


def per_device(features, weight, tile_values, tile_count, tile_cols, out_grad, relu_mask):
    row_tiles = tile_values.shape[0]
    slot_count = tile_values.shape[1]
    tile_size = tile_values.shape[2]
    feature_width = features.shape[2]
    blk_size = lax.axis_size("blk")
    rep_size = lax.axis_size("rep")
    community = blk_size * row_tiles
    local_cols = tile_cols // (rep_size * row_tiles) * row_tiles + tile_cols % row_tiles
    in_use = lax.broadcasted_iota(jnp.int32, (row_tiles, slot_count), 1) < tile_count[:, None]
    member_ids = lax.broadcasted_iota(jnp.int32, (row_tiles, slot_count, community), 2)
    one_hot = ((local_cols[:, :, None] == member_ids) & in_use[:, :, None]).astype(jnp.bfloat16)
    selected = jnp.einsum(
        "tsc,tsji->tcji", one_hot, tile_values, preferred_element_type=jnp.float32
    ).astype(jnp.bfloat16)
    gathered = lax.all_gather(features, "blk", axis=0, tiled=True)
    picked = gathered[local_cols]
    picked = jnp.where(in_use[:, :, None, None], picked, jnp.zeros((), jnp.bfloat16))
    partial_value = jnp.einsum(
        "tsji,tsjf->tif", tile_values, picked, preferred_element_type=jnp.float32
    )
    hidden = partial_value.astype(jnp.bfloat16)
    hidden_flat = hidden.reshape(-1, feature_width)
    linear = jnp.dot(hidden_flat, weight, preferred_element_type=jnp.float32)
    activated = jnp.maximum(linear, 0.0).astype(jnp.bfloat16).reshape(hidden.shape)
    grad_flat = out_grad.reshape(-1, feature_width)
    grad_term = lax.dot_general(
        hidden_flat, grad_flat, (((0,), (0,)), ((), ())), preferred_element_type=jnp.float32
    )
    node_count = row_tiles * blk_size * rep_size * tile_size
    weight_grad = _allreduce_doubling(grad_term, blk_size, rep_size) * (1.0 / math.sqrt(node_count))
    row_grad = lax.dot_general(
        grad_flat, weight, (((1,), (1,)), ((), ())), preferred_element_type=jnp.float32
    )
    row_grad = row_grad.astype(jnp.bfloat16).reshape(out_grad.shape)
    spread = lax.psum_scatter(
        jnp.einsum("tcji,tif->cjf", selected, row_grad, preferred_element_type=jnp.float32),
        "blk",
        scatter_dimension=0,
        tiled=True,
    )
    in_grad = (relu_mask.astype(jnp.float32) * spread).astype(jnp.bfloat16)
    return (activated, weight_grad, in_grad)


def _bits_order(blk_size, rep_size):
    rep_bits = [1 << b for b in range(rep_size.bit_length() - 1)]
    blk_bits = [rep_size << b for b in range(blk_size.bit_length() - 1)]
    return blk_bits[:1] + rep_bits + blk_bits[1:]


def _allreduce_doubling(x, blk_size, rep_size):
    total = blk_size * rep_size
    for mask in _bits_order(blk_size, rep_size):
        x = x + lax.ppermute(x, ("blk", "rep"), [(i, i ^ mask) for i in range(total)])
    return x


def _allreduce_halving(x, blk_size, rep_size):
    total = blk_size * rep_size
    me = lax.axis_index(("blk", "rep"))
    masks = _bits_order(blk_size, rep_size)
    flat = x.reshape(-1)
    for mask in masks:
        half = flat.shape[0] // 2
        upper = (me & mask) != 0
        lo, hi = flat[:half], flat[half:]
        keep = jnp.where(upper, hi, lo)
        send = jnp.where(upper, lo, hi)
        flat = keep + lax.ppermute(send, ("blk", "rep"), [(i, i ^ mask) for i in range(total)])
    for mask in reversed(masks):
        upper = (me & mask) != 0
        other = lax.ppermute(flat, ("blk", "rep"), [(i, i ^ mask) for i in range(total)])
        flat = jnp.concatenate([jnp.where(upper, other, flat), jnp.where(upper, flat, other)])
    return flat.reshape(x.shape)


def solution(mesh):
    placed = (
        P(("blk", "rep"), None, None),
        P(),
        P(("blk", "rep"), None, None, None),
        P(("blk", "rep")),
        P(("blk", "rep"), None),
        P(("blk", "rep"), None, None),
        P(("blk", "rep"), None, None),
    )
    return jax.shard_map(
        per_device,
        mesh=mesh,
        in_specs=placed,
        out_specs=(P(("blk", "rep"), None, None), P(), P(("blk", "rep"), None, None)),
        check_vma=False,
    )
```

```python
import math

import jax
import jax.numpy as jnp
from jax import lax
from jax.sharding import PartitionSpec as P


def per_device(features, weight, tile_values, tile_count, tile_cols, out_grad, relu_mask):
    row_tiles = tile_values.shape[0]
    slot_count = tile_values.shape[1]
    tile_size = tile_values.shape[2]
    feature_width = features.shape[2]
    blk_size = lax.axis_size("blk")
    rep_size = lax.axis_size("rep")
    community = blk_size * row_tiles
    local_cols = tile_cols // (rep_size * row_tiles) * row_tiles + tile_cols % row_tiles
    in_use = lax.broadcasted_iota(jnp.int32, (row_tiles, slot_count), 1) < tile_count[:, None]
    member_ids = lax.broadcasted_iota(jnp.int32, (row_tiles, slot_count, community), 2)
    one_hot = ((local_cols[:, :, None] == member_ids) & in_use[:, :, None]).astype(jnp.bfloat16)
    selected = jnp.einsum(
        "tsc,tsji->tcji", one_hot, tile_values, preferred_element_type=jnp.float32
    ).astype(jnp.bfloat16)
    gathered = lax.all_gather(features, "blk", axis=0, tiled=True)
    picked = gathered[local_cols]
    picked = jnp.where(in_use[:, :, None, None], picked, jnp.zeros((), jnp.bfloat16))
    partial_value = jnp.einsum(
        "tsji,tsjf->tif", tile_values, picked, preferred_element_type=jnp.float32
    )
    hidden = partial_value.astype(jnp.bfloat16)
    hidden_flat = hidden.reshape(-1, feature_width)
    linear = jnp.dot(hidden_flat, weight, preferred_element_type=jnp.float32)
    activated = jnp.maximum(linear, 0.0).astype(jnp.bfloat16).reshape(hidden.shape)
    grad_flat = out_grad.reshape(-1, feature_width)
    grad_term = lax.dot_general(
        hidden_flat, grad_flat, (((0,), (0,)), ((), ())), preferred_element_type=jnp.float32
    )
    node_count = row_tiles * blk_size * rep_size * tile_size
    weight_grad = _allreduce_doubling(grad_term, blk_size, rep_size) * (1.0 / math.sqrt(node_count))
    row_grad = lax.dot_general(
        grad_flat, weight, (((1,), (1,)), ((), ())), preferred_element_type=jnp.float32
    )
    row_grad = row_grad.astype(jnp.bfloat16).reshape(out_grad.shape)
    spread = lax.psum_scatter(
        jnp.einsum("tcji,tif->cjf", selected, row_grad, preferred_element_type=jnp.float32),
        "blk",
        scatter_dimension=0,
        tiled=True,
    )
    in_grad = (relu_mask.astype(jnp.float32) * spread).astype(jnp.bfloat16)
    return (activated, weight_grad, in_grad)


def _bits_order(blk_size, rep_size):
    rep_bits = [1 << b for b in range(rep_size.bit_length() - 1)]
    blk_bits = [rep_size << b for b in range(blk_size.bit_length() - 1)]
    return blk_bits[:1] + rep_bits + blk_bits[1:]


def _allreduce_doubling(x, blk_size, rep_size):
    total = blk_size * rep_size
    me = lax.axis_index(("blk", "rep"))
    masks = _bits_order(blk_size, rep_size)
    flat = x.reshape(-1)
    half = flat.shape[0] // 2
    upper = (me & masks[0]) != 0
    keep = jnp.where(upper, flat[half:], flat[:half])
    send = jnp.where(upper, flat[:half], flat[half:])
    flat = keep + lax.ppermute(send, ("blk", "rep"), [(i, i ^ masks[0]) for i in range(total)])
    for mask in masks[1:]:
        flat = flat + lax.ppermute(flat, ("blk", "rep"), [(i, i ^ mask) for i in range(total)])
    other = lax.ppermute(flat, ("blk", "rep"), [(i, i ^ masks[0]) for i in range(total)])
    flat = jnp.concatenate([jnp.where(upper, other, flat), jnp.where(upper, flat, other)])
    return flat.reshape(x.shape)


def _allreduce_halving(x, blk_size, rep_size):
    total = blk_size * rep_size
    me = lax.axis_index(("blk", "rep"))
    masks = _bits_order(blk_size, rep_size)
    flat = x.reshape(-1)
    for mask in masks:
        half = flat.shape[0] // 2
        upper = (me & mask) != 0
        lo, hi = flat[:half], flat[half:]
        keep = jnp.where(upper, hi, lo)
        send = jnp.where(upper, lo, hi)
        flat = keep + lax.ppermute(send, ("blk", "rep"), [(i, i ^ mask) for i in range(total)])
    for mask in reversed(masks):
        upper = (me & mask) != 0
        other = lax.ppermute(flat, ("blk", "rep"), [(i, i ^ mask) for i in range(total)])
        flat = jnp.concatenate([jnp.where(upper, other, flat), jnp.where(upper, flat, other)])
    return flat.reshape(x.shape)


def solution(mesh):
    placed = (
        P(("blk", "rep"), None, None),
        P(),
        P(("blk", "rep"), None, None, None),
        P(("blk", "rep")),
        P(("blk", "rep"), None),
        P(("blk", "rep"), None, None),
        P(("blk", "rep"), None, None),
    )
    return jax.shard_map(
        per_device,
        mesh=mesh,
        in_specs=placed,
        out_specs=(P(("blk", "rep"), None, None), P(), P(("blk", "rep"), None, None)),
        check_vma=False,
    )
```

```python
import math

import jax
import jax.numpy as jnp
from jax import lax
from jax.sharding import PartitionSpec as P


def per_device(features, weight, tile_values, tile_count, tile_cols, out_grad, relu_mask):
    row_tiles = tile_values.shape[0]
    slot_count = tile_values.shape[1]
    tile_size = tile_values.shape[2]
    feature_width = features.shape[2]
    blk_size = lax.axis_size("blk")
    rep_size = lax.axis_size("rep")
    community = blk_size * row_tiles
    local_cols = tile_cols // (rep_size * row_tiles) * row_tiles + tile_cols % row_tiles
    in_use = lax.broadcasted_iota(jnp.int32, (row_tiles, slot_count), 1) < tile_count[:, None]
    member_ids = lax.broadcasted_iota(jnp.int32, (row_tiles, slot_count, community), 2)
    one_hot = ((local_cols[:, :, None] == member_ids) & in_use[:, :, None]).astype(jnp.bfloat16)
    selected = jnp.einsum(
        "tsc,tsji->tcji", one_hot, tile_values, preferred_element_type=jnp.float32
    ).astype(jnp.bfloat16)
    gathered = lax.all_gather(features, "blk", axis=0, tiled=True)
    picked = gathered[local_cols]
    picked = jnp.where(in_use[:, :, None, None], picked, jnp.zeros((), jnp.bfloat16))
    partial_value = jnp.einsum(
        "tsji,tsjf->tif", tile_values, picked, preferred_element_type=jnp.float32
    )
    hidden = partial_value.astype(jnp.bfloat16)
    hidden_flat = hidden.reshape(-1, feature_width)
    linear = jnp.dot(hidden_flat, weight, preferred_element_type=jnp.float32)
    activated = jnp.maximum(linear, 0.0).astype(jnp.bfloat16).reshape(hidden.shape)
    grad_flat = out_grad.reshape(-1, feature_width)
    grad_term = lax.dot_general(
        hidden_flat, grad_flat, (((0,), (0,)), ((), ())), preferred_element_type=jnp.float32
    )
    node_count = row_tiles * blk_size * rep_size * tile_size
    weight_grad = _allreduce_doubling(grad_term, blk_size, rep_size) * (1.0 / math.sqrt(node_count))
    row_grad = lax.dot_general(
        grad_flat, weight, (((1,), (1,)), ((), ())), preferred_element_type=jnp.float32
    )
    row_grad = row_grad.astype(jnp.bfloat16).reshape(out_grad.shape)
    spread = lax.psum_scatter(
        jnp.einsum("tcji,tif->cjf", selected, row_grad, preferred_element_type=jnp.float32),
        "blk",
        scatter_dimension=0,
        tiled=True,
    )
    in_grad = (relu_mask.astype(jnp.float32) * spread).astype(jnp.bfloat16)
    return (activated, weight_grad, in_grad)


def _bits_order(blk_size, rep_size):
    rep_bits = [1 << b for b in range(rep_size.bit_length() - 1)]
    blk_bits = [rep_size << b for b in range(blk_size.bit_length() - 1)]
    side = len(rep_bits) // 2
    near = [blk_bits[0], rep_bits[0], rep_bits[side], blk_bits[1]]
    far = rep_bits[1:side] + rep_bits[side + 1:] + blk_bits[2:]
    return near[:2], near[2:] + far


def _allreduce_doubling(x, blk_size, rep_size):
    total = blk_size * rep_size
    me = lax.axis_index(("blk", "rep"))
    halving, doubling = _bits_order(blk_size, rep_size)
    flat = x.reshape(-1)
    for mask in halving:
        half = flat.shape[0] // 2
        upper = (me & mask) != 0
        keep = jnp.where(upper, flat[half:], flat[:half])
        send = jnp.where(upper, flat[:half], flat[half:])
        flat = keep + lax.ppermute(send, ("blk", "rep"), [(i, i ^ mask) for i in range(total)])
    for mask in doubling:
        flat = flat + lax.ppermute(flat, ("blk", "rep"), [(i, i ^ mask) for i in range(total)])
    for mask in reversed(halving):
        upper = (me & mask) != 0
        other = lax.ppermute(flat, ("blk", "rep"), [(i, i ^ mask) for i in range(total)])
        flat = jnp.concatenate([jnp.where(upper, other, flat), jnp.where(upper, flat, other)])
    return flat.reshape(x.shape)


def solution(mesh):
    placed = (
        P(("blk", "rep"), None, None),
        P(),
        P(("blk", "rep"), None, None, None),
        P(("blk", "rep")),
        P(("blk", "rep"), None),
        P(("blk", "rep"), None, None),
        P(("blk", "rep"), None, None),
    )
    return jax.shard_map(
        per_device,
        mesh=mesh,
        in_specs=placed,
        out_specs=(P(("blk", "rep"), None, None), P(), P(("blk", "rep"), None, None)),
        check_vma=False,
    )
```

```python
import math

import jax
import jax.numpy as jnp
from jax import lax
from jax.sharding import PartitionSpec as P


def per_device(features, weight, tile_values, tile_count, tile_cols, out_grad, relu_mask):
    row_tiles = tile_values.shape[0]
    slot_count = tile_values.shape[1]
    tile_size = tile_values.shape[2]
    feature_width = features.shape[2]
    blk_size = lax.axis_size("blk")
    rep_size = lax.axis_size("rep")
    community = blk_size * row_tiles
    local_cols = tile_cols // (rep_size * row_tiles) * row_tiles + tile_cols % row_tiles
    in_use = lax.broadcasted_iota(jnp.int32, (row_tiles, slot_count), 1) < tile_count[:, None]
    member_ids = lax.broadcasted_iota(jnp.int32, (row_tiles, slot_count, community), 2)
    one_hot = ((local_cols[:, :, None] == member_ids) & in_use[:, :, None]).astype(jnp.bfloat16)
    selected = jnp.einsum(
        "tsc,tsji->tcji", one_hot, tile_values, preferred_element_type=jnp.float32
    ).astype(jnp.bfloat16)
    gathered = lax.all_gather(features, "blk", axis=0, tiled=True)
    partial_value = jnp.einsum(
        "tcji,cjf->tif", selected, gathered, preferred_element_type=jnp.float32
    )
    hidden = partial_value.astype(jnp.bfloat16)
    hidden_flat = hidden.reshape(-1, feature_width)
    linear = jnp.dot(hidden_flat, weight, preferred_element_type=jnp.float32)
    activated = jnp.maximum(linear, 0.0).astype(jnp.bfloat16).reshape(hidden.shape)
    grad_flat = out_grad.reshape(-1, feature_width)
    grad_term = lax.dot_general(
        hidden_flat, grad_flat, (((0,), (0,)), ((), ())), preferred_element_type=jnp.float32
    )
    node_count = row_tiles * blk_size * rep_size * tile_size
    weight_grad = _allreduce_doubling(grad_term, blk_size, rep_size) * (1.0 / math.sqrt(node_count))
    row_grad = lax.dot_general(
        grad_flat, weight, (((1,), (1,)), ((), ())), preferred_element_type=jnp.float32
    )
    row_grad = row_grad.astype(jnp.bfloat16).reshape(out_grad.shape)
    spread = lax.psum_scatter(
        jnp.einsum("tcji,tif->cjf", selected, row_grad, preferred_element_type=jnp.float32),
        "blk",
        scatter_dimension=0,
        tiled=True,
    )
    in_grad = (relu_mask.astype(jnp.float32) * spread).astype(jnp.bfloat16)
    return (activated, weight_grad, in_grad)


def _bits_order(blk_size, rep_size):
    rep_bits = [1 << b for b in range(rep_size.bit_length() - 1)]
    blk_bits = [rep_size << b for b in range(blk_size.bit_length() - 1)]
    side = len(rep_bits) // 2
    near = [blk_bits[0], rep_bits[0], rep_bits[side], blk_bits[1]]
    far = rep_bits[1:side] + rep_bits[side + 1:] + blk_bits[2:]
    return near[:2], near[2:] + far


def _allreduce_doubling(x, blk_size, rep_size):
    total = blk_size * rep_size
    me = lax.axis_index(("blk", "rep"))
    halving, doubling = _bits_order(blk_size, rep_size)
    flat = x.reshape(-1)
    for mask in halving:
        half = flat.shape[0] // 2
        upper = (me & mask) != 0
        keep = jnp.where(upper, flat[half:], flat[:half])
        send = jnp.where(upper, flat[:half], flat[half:])
        flat = keep + lax.ppermute(send, ("blk", "rep"), [(i, i ^ mask) for i in range(total)])
    for mask in doubling:
        flat = flat + lax.ppermute(flat, ("blk", "rep"), [(i, i ^ mask) for i in range(total)])
    for mask in reversed(halving):
        upper = (me & mask) != 0
        other = lax.ppermute(flat, ("blk", "rep"), [(i, i ^ mask) for i in range(total)])
        flat = jnp.concatenate([jnp.where(upper, other, flat), jnp.where(upper, flat, other)])
    return flat.reshape(x.shape)


def solution(mesh):
    placed = (
        P(("blk", "rep"), None, None),
        P(),
        P(("blk", "rep"), None, None, None),
        P(("blk", "rep")),
        P(("blk", "rep"), None),
        P(("blk", "rep"), None, None),
        P(("blk", "rep"), None, None),
    )
    return jax.shard_map(
        per_device,
        mesh=mesh,
        in_specs=placed,
        out_specs=(P(("blk", "rep"), None, None), P(), P(("blk", "rep"), None, None)),
        check_vma=False,
    )
```

```python
import math

import jax
import jax.numpy as jnp
from jax import lax
from jax.sharding import PartitionSpec as P


def per_device(features, weight, tile_values, tile_count, tile_cols, out_grad, relu_mask):
    row_tiles = tile_values.shape[0]
    slot_count = tile_values.shape[1]
    tile_size = tile_values.shape[2]
    feature_width = features.shape[2]
    blk_size = lax.axis_size("blk")
    rep_size = lax.axis_size("rep")
    community = blk_size * row_tiles
    local_cols = tile_cols // (rep_size * row_tiles) * row_tiles + tile_cols % row_tiles
    in_use = lax.broadcasted_iota(jnp.int32, (row_tiles, slot_count), 1) < tile_count[:, None]
    member_ids = lax.broadcasted_iota(jnp.int32, (row_tiles, slot_count, community), 2)
    one_hot = ((local_cols[:, :, None] == member_ids) & in_use[:, :, None]).astype(jnp.bfloat16)
    selected = jnp.einsum(
        "tsc,tsji->tcji", one_hot, tile_values, preferred_element_type=jnp.float32
    ).astype(jnp.bfloat16)
    gathered = lax.all_gather(features, "blk", axis=0, tiled=True)
    partial_value = jnp.einsum(
        "tcji,cjf->tif", selected, gathered, preferred_element_type=jnp.float32
    )
    hidden = partial_value.astype(jnp.bfloat16)
    hidden_flat = hidden.reshape(-1, feature_width)
    linear = jnp.dot(hidden_flat, weight, preferred_element_type=jnp.float32)
    activated = jnp.maximum(linear, 0.0).astype(jnp.bfloat16).reshape(hidden.shape)
    grad_flat = out_grad.reshape(-1, feature_width)
    grad_term = lax.dot_general(
        hidden_flat, grad_flat, (((0,), (0,)), ((), ())), preferred_element_type=jnp.float32
    )
    node_count = row_tiles * blk_size * rep_size * tile_size
    weight_grad = _allreduce_doubling(grad_term, blk_size, rep_size) * (1.0 / math.sqrt(node_count))
    row_grad = lax.dot_general(
        grad_flat, weight, (((1,), (1,)), ((), ())), preferred_element_type=jnp.float32
    )
    row_grad = row_grad.astype(jnp.bfloat16).reshape(out_grad.shape)
    spread = lax.psum_scatter(
        jnp.einsum("tcji,tif->cjf", selected, row_grad, preferred_element_type=jnp.float32).astype(jnp.bfloat16),
        "blk",
        scatter_dimension=0,
        tiled=True,
    )
    in_grad = (relu_mask.astype(jnp.float32) * spread).astype(jnp.bfloat16)
    return (activated, weight_grad, in_grad)


def _bits_order(blk_size, rep_size):
    rep_bits = [1 << b for b in range(rep_size.bit_length() - 1)]
    blk_bits = [rep_size << b for b in range(blk_size.bit_length() - 1)]
    side = len(rep_bits) // 2
    near = [blk_bits[0], rep_bits[0], rep_bits[side], blk_bits[1]]
    far = rep_bits[1:side] + rep_bits[side + 1:] + blk_bits[2:]
    return near[:2], near[2:] + far


def _allreduce_doubling(x, blk_size, rep_size):
    total = blk_size * rep_size
    me = lax.axis_index(("blk", "rep"))
    halving, doubling = _bits_order(blk_size, rep_size)
    flat = x.reshape(-1)
    for mask in halving:
        half = flat.shape[0] // 2
        upper = (me & mask) != 0
        keep = jnp.where(upper, flat[half:], flat[:half])
        send = jnp.where(upper, flat[:half], flat[half:])
        flat = keep + lax.ppermute(send, ("blk", "rep"), [(i, i ^ mask) for i in range(total)])
    for mask in doubling:
        flat = flat + lax.ppermute(flat, ("blk", "rep"), [(i, i ^ mask) for i in range(total)])
    for mask in reversed(halving):
        upper = (me & mask) != 0
        other = lax.ppermute(flat, ("blk", "rep"), [(i, i ^ mask) for i in range(total)])
        flat = jnp.concatenate([jnp.where(upper, other, flat), jnp.where(upper, flat, other)])
    return flat.reshape(x.shape)


def solution(mesh):
    placed = (
        P(("blk", "rep"), None, None),
        P(),
        P(("blk", "rep"), None, None, None),
        P(("blk", "rep")),
        P(("blk", "rep"), None),
        P(("blk", "rep"), None, None),
        P(("blk", "rep"), None, None),
    )
    return jax.shard_map(
        per_device,
        mesh=mesh,
        in_specs=placed,
        out_specs=(P(("blk", "rep"), None, None), P(), P(("blk", "rep"), None, None)),
        check_vma=False,
    )
```

```python
import math

import jax
import jax.numpy as jnp
from jax import lax
from jax.sharding import PartitionSpec as P


def per_device(features, weight, tile_values, tile_count, tile_cols, out_grad, relu_mask):
    row_tiles = tile_values.shape[0]
    slot_count = tile_values.shape[1]
    tile_size = tile_values.shape[2]
    feature_width = features.shape[2]
    blk_size = lax.axis_size("blk")
    rep_size = lax.axis_size("rep")
    community = blk_size * row_tiles
    local_cols = tile_cols // (rep_size * row_tiles) * row_tiles + tile_cols % row_tiles
    in_use = lax.broadcasted_iota(jnp.int32, (row_tiles, slot_count), 1) < tile_count[:, None]
    member_ids = lax.broadcasted_iota(jnp.int32, (row_tiles, slot_count, community), 2)
    one_hot = ((local_cols[:, :, None] == member_ids) & in_use[:, :, None]).astype(jnp.bfloat16)
    selected = jnp.einsum(
        "tsc,tsji->tcji", one_hot, tile_values, preferred_element_type=jnp.float32
    ).astype(jnp.bfloat16)
    gathered = lax.all_gather(features, "blk", axis=0, tiled=True)
    partial_value = jnp.einsum(
        "tcji,cjf->tif", selected, gathered, preferred_element_type=jnp.float32
    )
    hidden = partial_value.astype(jnp.bfloat16)
    hidden_flat = hidden.reshape(-1, feature_width)
    linear = jnp.dot(hidden_flat, weight, preferred_element_type=jnp.float32)
    activated = jnp.maximum(linear, 0.0).astype(jnp.bfloat16).reshape(hidden.shape)
    grad_flat = out_grad.reshape(-1, feature_width)
    grad_term = lax.dot_general(
        hidden_flat, grad_flat, (((0,), (0,)), ((), ())), preferred_element_type=jnp.float32
    )
    node_count = row_tiles * blk_size * rep_size * tile_size
    weight_grad = _allreduce_doubling(grad_term * (1.0 / math.sqrt(node_count)), blk_size, rep_size)
    row_grad = lax.dot_general(
        grad_flat, weight, (((1,), (1,)), ((), ())), preferred_element_type=jnp.float32
    )
    row_grad = row_grad.astype(jnp.bfloat16).reshape(out_grad.shape)
    spread = lax.psum_scatter(
        jnp.einsum("tcji,tif->cjf", selected, row_grad, preferred_element_type=jnp.float32),
        "blk",
        scatter_dimension=0,
        tiled=True,
    )
    in_grad = (relu_mask.astype(jnp.float32) * spread).astype(jnp.bfloat16)
    return (activated, weight_grad, in_grad)


def _bits_order(blk_size, rep_size):
    rep_bits = [1 << b for b in range(rep_size.bit_length() - 1)]
    blk_bits = [rep_size << b for b in range(blk_size.bit_length() - 1)]
    side = len(rep_bits) // 2
    near = [blk_bits[0], rep_bits[0], rep_bits[side], blk_bits[1]]
    far = rep_bits[1:side] + rep_bits[side + 1:] + blk_bits[2:]
    return near[:2], near[2:] + far


def _allreduce_doubling(x, blk_size, rep_size):
    total = blk_size * rep_size
    me = lax.axis_index(("blk", "rep"))
    halving, doubling = _bits_order(blk_size, rep_size)
    flat = x.reshape(-1)
    for mask in halving:
        half = flat.shape[0] // 2
        upper = (me & mask) != 0
        keep = jnp.where(upper, flat[half:], flat[:half])
        send = jnp.where(upper, flat[:half], flat[half:])
        flat = keep + lax.ppermute(send, ("blk", "rep"), [(i, i ^ mask) for i in range(total)])
    for mask in doubling:
        flat = flat + lax.ppermute(flat, ("blk", "rep"), [(i, i ^ mask) for i in range(total)])
    for mask in reversed(halving):
        upper = (me & mask) != 0
        other = lax.ppermute(flat, ("blk", "rep"), [(i, i ^ mask) for i in range(total)])
        flat = jnp.concatenate([jnp.where(upper, other, flat), jnp.where(upper, flat, other)])
    return flat.reshape(x.shape)


def solution(mesh):
    placed = (
        P(("blk", "rep"), None, None),
        P(),
        P(("blk", "rep"), None, None, None),
        P(("blk", "rep")),
        P(("blk", "rep"), None),
        P(("blk", "rep"), None, None),
        P(("blk", "rep"), None, None),
    )
    return jax.shard_map(
        per_device,
        mesh=mesh,
        in_specs=placed,
        out_specs=(P(("blk", "rep"), None, None), P(), P(("blk", "rep"), None, None)),
        check_vma=False,
    )
```
